32 devices in a mesh: row: 8 (over z, core), col: 4 (over y, x).
Axes of the slice: x: 2, y: 2, z: 4, core: 2. Of those that a mesh axis runs over, the one named last changes fastest.
Arguments:
- amplitudes: float32 [1024, 2048], P(('row', 'col')), may hold values from -6 to 6
- integral_tiles: float32 [1024, 128, 128], P(('row', 'col')), may hold values from -0.125 to 0.125
- tile_cd: int32 [1024], P(('row', 'col')), may hold values from 0 to 15, as said below
- tile_ab: int32 [1024], P(('row', 'col')), may hold values from 0 to 15
- tile_count: int32 [32], P(('row', 'col')), may hold values from 16 to 32, as said below
Outputs:
- residual: float32 [1024, 65536], P(None, ('row', 'col'))
The draws below stay inside these ranges and needn't reach their ends.
Inputs may be any that keep to these rules, and one draw needn't show every extreme that they name: Every cd block carries one D2h irrep label of 8, the same for all sets, each label on 2 cd blocks; within a set every ab block carries a label likewise, each on 2 ab blocks; the 32 slots of a set hold exactly the (tile_cd, tile_ab) pairs whose labels are equal, each once, in an order that differs from set to set. `tile_count`: in every draw one set has all 32 slots live and another has 16.
All inputs are finite; a program needn't handle non-finite values.
Results may differ from the reference program's by a relative error of at most 0.0003.
Values sent between devices are 32-bit elements; how exact they have to be, the bound alone decides.
No kernel may reach another device: no remote copies, remote signals or barrier semaphores. Data moves between devices by JAX's collectives and lax.ppermute only.
A program may use at most 128 MiB of HBM per device.

```python
import jax
import jax.numpy as jnp
from jax import lax

OPB = 1024
BLK = 128
AB_DEV = 2048
CD = 2048
SETS = 32
SLOTS = 32
TILES = 1024


def tile_plan(key):
    set_total = TILES // SLOTS
    cd_blocks = CD // BLK
    ab_blocks = AB_DEV // BLK
    cd_per = cd_blocks // 8
    ab_per = ab_blocks // 8
    cd_perm = jax.random.permutation(jax.random.fold_in(key, 5), cd_blocks).astype(jnp.int32)
    irrep = jnp.arange(8, dtype=jnp.int32)[:, None, None]
    cd_step = jnp.arange(cd_per, dtype=jnp.int32)[None, :, None]
    ab_step = jnp.arange(ab_per, dtype=jnp.int32)[None, None, :]
    cd_pos = jnp.broadcast_to(irrep + 8 * cd_step, (8, cd_per, ab_per)).reshape(-1)
    ab_pos = jnp.broadcast_to(irrep + 8 * ab_step, (8, cd_per, ab_per)).reshape(-1)

    def one_set(sub_key):
        ab_perm = jax.random.permutation(jax.random.fold_in(sub_key, 1), ab_blocks).astype(jnp.int32)
        order = jax.random.permutation(jax.random.fold_in(sub_key, 2), SLOTS).astype(jnp.int32)
        set_cd = cd_perm[cd_pos][order]
        set_ab = ab_perm[ab_pos][order]
        return (set_cd, set_ab)
    key_list = jax.random.split(jax.random.fold_in(key, 7), set_total)
    all_cd, all_ab = jax.vmap(one_set)(key_list)
    counts = jax.random.randint(jax.random.fold_in(key, 11), (set_total,), SLOTS // 2, SLOTS + 1)
    full_set = jax.random.randint(jax.random.fold_in(key, 13), (), 0, set_total)
    half_set = (full_set + 1 + jax.random.randint(jax.random.fold_in(key, 17), (), 0, set_total - 1)) % set_total
    group_index = jnp.arange(set_total, dtype=jnp.int32)
    counts = jnp.where(group_index == full_set, SLOTS, counts)
    counts = jnp.where(group_index == half_set, SLOTS // 2, counts)
    return (all_cd.astype(jnp.int32), all_ab.astype(jnp.int32), counts.astype(jnp.int32))


def draw_tile_cd(key, part):
    all_cd, all_ab, counts = tile_plan(key)
    return all_cd.reshape(-1).astype(jnp.int32)


def draw_tile_ab(key, part):
    all_cd, all_ab, counts = tile_plan(key)
    return all_ab.reshape(-1).astype(jnp.int32)


def draw_tile_count(key, part):
    all_cd, all_ab, counts = tile_plan(key)
    return counts


def shard_levels(rng, shape, pieces, least, high):
    def one(dim, blocks):
        steps = jax.random.uniform(jax.random.fold_in(jax.random.fold_in(rng, 6), dim), (blocks,), jnp.float32, least / len(pieces), high / len(pieces))
        return jnp.repeat(jnp.exp(steps), shape[dim] // blocks).reshape((-1,) + (1,) * (len(shape) - dim - 1))

    loudness = one(*pieces[0])
    for cut in pieces[1:]:
        loudness = loudness * one(*cut)
    return loudness


def gaussian(stream_key, dims, deviation, most, cuts=(), held_as=jnp.bfloat16):
    loudness = shard_levels(stream_key, dims, cuts, -0.22, 0.18) if cuts else 1.0
    values = jax.random.normal(stream_key, dims, jnp.float32) * deviation * loudness
    return jnp.minimum(jnp.maximum(values, -most), most).astype(held_as)


def setup_inputs(seed: int = 0) -> dict:
    streams_of = jax.random.split(jax.random.key(seed), 6)
    return {
        "amplitudes": gaussian(streams_of[0], (OPB, CD), 1.0, 6.0, ((0, 32),), jnp.float32),
        "integral_tiles": gaussian(streams_of[1], (TILES, BLK, BLK), CD ** -0.5, 0.125, ((0, 32),), jnp.float32),
        "tile_cd": draw_tile_cd(jax.random.fold_in(streams_of[5], 71), 0),
        "tile_ab": draw_tile_ab(jax.random.fold_in(streams_of[5], 71), 0),
        "tile_count": draw_tile_count(jax.random.fold_in(streams_of[5], 71), 0),
    }


def dense_block(group_tiles, set_cd, set_ab, nonempty_count):
    cd_blocks = CD // BLK
    ab_blocks = AB_DEV // BLK
    bucket_index = jnp.arange(SLOTS, dtype=jnp.int32)
    active_flags = (bucket_index < nonempty_count).astype(jnp.float32)
    packed_location = (set_cd * ab_blocks + set_ab).astype(jnp.int32)
    stacked_blocks = jnp.zeros((cd_blocks * ab_blocks, BLK, BLK), jnp.float32)
    stacked_blocks = stacked_blocks.at[packed_location].add(group_tiles * active_flags[:, None, None])
    return stacked_blocks.reshape(cd_blocks, ab_blocks, BLK, BLK).transpose(0, 2, 1, 3).reshape(CD, AB_DEV)


def reference(amplitudes, integral_tiles, tile_cd, tile_ab, tile_count):
    def one_set(inputs):
        group_tiles, set_cd, set_ab, nonempty_count = inputs
        integrals = dense_block(group_tiles, set_cd, set_ab, nonempty_count)
        return jnp.dot(amplitudes, integrals, precision=lax.Precision.HIGHEST, preferred_element_type=jnp.float32)

    blocks = lax.map(one_set, (integral_tiles.reshape(SETS, SLOTS, BLK, BLK), tile_cd.reshape(SETS, SLOTS), tile_ab.reshape(SETS, SLOTS), tile_count))
    return blocks.transpose(1, 0, 2).reshape(OPB, SETS * AB_DEV)
```

```python
import jax
import jax.numpy as jnp
from jax import lax
from jax.experimental import pallas as pl
from jax.experimental.pallas import tpu as pltpu
from jax.sharding import PartitionSpec as P

BLK = 128
AB_DEV = 2048
SLOTS = 32


def ladder_kernel(order_ref, cd_ref, live_ref, amp_ref, tile_ref, out_ref):
    k = pl.program_id(1)
    idx = pl.program_id(0) * pl.num_programs(1) + k

    @pl.when(k == 0)
    def _():
        out_ref[...] = jnp.zeros_like(out_ref)

    @pl.when(live_ref[idx] > 0)
    def _():
        out_ref[...] += jnp.dot(
            amp_ref[...],
            tile_ref[0],
            precision=lax.Precision.HIGHEST,
            preferred_element_type=jnp.float32,
        )


def sparse_ladder(amps, tiles, tile_cd, tile_ab, count):
    rows = amps.shape[0]
    ab_blocks = AB_DEV // BLK
    per_ab = SLOTS // ab_blocks
    order = jnp.argsort(tile_ab, stable=True).astype(jnp.int32)
    cd_sorted = tile_cd[order].astype(jnp.int32)
    live_sorted = (order < count).astype(jnp.int32)
    grid_spec = pltpu.PrefetchScalarGridSpec(
        num_scalar_prefetch=3,
        grid=(ab_blocks, per_ab),
        in_specs=[
            pl.BlockSpec((rows, BLK), lambda j, k, o, c, l: (0, c[j * per_ab + k])),
            pl.BlockSpec((1, BLK, BLK), lambda j, k, o, c, l: (o[j * per_ab + k], 0, 0)),
        ],
        out_specs=pl.BlockSpec((rows, BLK), lambda j, k, o, c, l: (0, j)),
    )
    return pl.pallas_call(
        ladder_kernel,
        grid_spec=grid_spec,
        out_shape=jax.ShapeDtypeStruct((rows, AB_DEV), jnp.float32),
        compiler_params=pltpu.CompilerParams(dimension_semantics=("arbitrary", "arbitrary")),
    )(order, cd_sorted, live_sorted, amps, tiles)


def on_device(amplitudes, integral_tiles, tile_cd, tile_ab, tile_count):
    amps = lax.all_gather(amplitudes, ("row", "col"), axis=0, tiled=True)
    return sparse_ladder(amps, integral_tiles, tile_cd, tile_ab, tile_count[0])


def solution(mesh):
    placed = (
        P(("row", "col"), None),
        P(("row", "col"), None, None),
        P(("row", "col")),
        P(("row", "col")),
        P(("row", "col")),
    )
    return jax.shard_map(
        on_device, mesh=mesh, in_specs=placed, out_specs=P(None, ("row", "col")), check_vma=False
    )
```

```python
import jax
import jax.numpy as jnp
from jax import lax
from jax.experimental import pallas as pl
from jax.experimental.pallas import tpu as pltpu
from jax.sharding import PartitionSpec as P

BLK = 128
AB_DEV = 2048
SLOTS = 32
ROW_TILE = 256


def split_dot(a, b):
    a_hi = a.astype(jnp.bfloat16)
    a_lo = (a - a_hi.astype(jnp.float32)).astype(jnp.bfloat16)
    b_hi = b.astype(jnp.bfloat16)
    b_lo = (b - b_hi.astype(jnp.float32)).astype(jnp.bfloat16)

    def dot(x, y):
        return jnp.dot(x, y, preferred_element_type=jnp.float32)

    return dot(a_hi, b_hi) + (dot(a_hi, b_lo) + dot(a_lo, b_hi))


def make_kernel(ab_blocks, per_ab):
    def ladder_kernel(order_ref, cd_ref, live_ref, amp_ref, tile_ref, out_ref):
        for j in range(ab_blocks):
            acc = None
            for k in range(per_ab):
                idx = j * per_ab + k
                part = split_dot(amp_ref[cd_ref[idx]], tile_ref[order_ref[idx]])
                part = jnp.where(live_ref[idx] > 0, part, 0.0)
                acc = part if acc is None else acc + part
            out_ref[:, j * BLK:(j + 1) * BLK] = acc

    return ladder_kernel


def slot_tables(tile_cd, tile_ab, count):
    n = tile_ab.shape[0]
    slot = jnp.arange(n, dtype=jnp.int32)
    key = tile_ab.astype(jnp.int32) * n + slot
    rank = jnp.sum((key[None, :] < key[:, None]).astype(jnp.int32), axis=1)
    hit = rank[None, :] == slot[:, None]
    order = jnp.sum(jnp.where(hit, slot[None, :], 0), axis=1)
    cd_sorted = jnp.sum(jnp.where(hit, tile_cd[None, :].astype(jnp.int32), 0), axis=1)
    live_sorted = (order < count).astype(jnp.int32)
    return order, cd_sorted, live_sorted


def sparse_ladder(amp3, tiles, tile_cd, tile_ab, count):
    ncd, rows, _ = amp3.shape
    ab_blocks = AB_DEV // BLK
    per_ab = SLOTS // ab_blocks
    order, cd_sorted, live_sorted = slot_tables(tile_cd, tile_ab, count)
    grid_spec = pltpu.PrefetchScalarGridSpec(
        num_scalar_prefetch=3,
        grid=(rows // ROW_TILE,),
        in_specs=[
            pl.BlockSpec((ncd, ROW_TILE, BLK), lambda i, o, c, l: (0, i, 0)),
            pl.BlockSpec(tiles.shape, lambda i, o, c, l: (0, 0, 0)),
        ],
        out_specs=pl.BlockSpec((ROW_TILE, AB_DEV), lambda i, o, c, l: (i, 0)),
    )
    return pl.pallas_call(
        make_kernel(ab_blocks, per_ab),
        grid_spec=grid_spec,
        out_shape=jax.ShapeDtypeStruct((rows, AB_DEV), jnp.float32),
    )(order, cd_sorted, live_sorted, amp3, tiles)


def on_device(amplitudes, integral_tiles, tile_cd, tile_ab, tile_count):
    rows, cd = amplitudes.shape
    local = amplitudes.reshape(rows, cd // BLK, BLK).transpose(1, 0, 2)
    amp3 = lax.all_gather(local, ("row", "col"), axis=1, tiled=True)
    return sparse_ladder(amp3, integral_tiles, tile_cd, tile_ab, tile_count[0])


def solution(mesh):
    placed = (
        P(("row", "col"), None),
        P(("row", "col"), None, None),
        P(("row", "col")),
        P(("row", "col")),
        P(("row", "col")),
    )
    return jax.shard_map(
        on_device, mesh=mesh, in_specs=placed, out_specs=P(None, ("row", "col")), check_vma=False
    )
```

```python
import jax
import jax.numpy as jnp
from jax import lax
from jax.experimental import pallas as pl
from jax.experimental.pallas import tpu as pltpu
from jax.sharding import PartitionSpec as P

BLK = 128
AB_DEV = 2048
SLOTS = 32
ROW_TILE = 256


def split_f32(x):
    hi = x.astype(jnp.bfloat16)
    return hi, (x - hi.astype(jnp.float32)).astype(jnp.bfloat16)


def split_tiles(x):
    hi = lax.reduce_precision(x, exponent_bits=8, mantissa_bits=7)
    return hi.astype(jnp.bfloat16), (x - hi).astype(jnp.bfloat16)


def make_kernel(ncd, per_cd, ab_blocks):
    def dot(x, y):
        return jnp.dot(x, y, preferred_element_type=jnp.float32)

    def ladder_kernel(order_ref, ab_ref, live_ref, amp_ref, hi_ref, lo_ref, out_ref, acc_ref):
        acc_ref[...] = jnp.zeros_like(acc_ref)
        for c in range(ncd):
            a_hi, a_lo = split_f32(amp_ref[c])
            for k in range(per_cd):
                idx = c * per_cd + k

                @pl.when(live_ref[idx] > 0)
                def _():
                    s = order_ref[idx]
                    t_hi = hi_ref[s]
                    part = dot(a_hi, t_hi) + (dot(a_hi, lo_ref[s]) + dot(a_lo, t_hi))
                    acc_ref[ab_ref[idx]] += part

        for j in range(ab_blocks):
            out_ref[:, j * BLK:(j + 1) * BLK] = acc_ref[j]

    return ladder_kernel


def slot_tables(tile_cd, tile_ab, count):
    n = tile_cd.shape[0]
    slot = jnp.arange(n, dtype=jnp.int32)
    key = tile_cd.astype(jnp.int32) * n + slot
    rank = jnp.sum((key[None, :] < key[:, None]).astype(jnp.int32), axis=1)
    hit = rank[None, :] == slot[:, None]
    order = jnp.sum(jnp.where(hit, slot[None, :], 0), axis=1)
    ab_sorted = jnp.sum(jnp.where(hit, tile_ab[None, :].astype(jnp.int32), 0), axis=1)
    live_sorted = (order < count).astype(jnp.int32)
    return order, ab_sorted, live_sorted


def sparse_ladder(amp3, tiles, tile_cd, tile_ab, count):
    ncd, rows, _ = amp3.shape
    ab_blocks = AB_DEV // BLK
    per_cd = SLOTS // ncd
    order, ab_sorted, live_sorted = slot_tables(tile_cd, tile_ab, count)
    t_hi, t_lo = split_tiles(tiles)
    grid_spec = pltpu.PrefetchScalarGridSpec(
        num_scalar_prefetch=3,
        grid=(rows // ROW_TILE,),
        in_specs=[
            pl.BlockSpec((ncd, ROW_TILE, BLK), lambda i, o, a, l: (0, i, 0)),
            pl.BlockSpec(t_hi.shape, lambda i, o, a, l: (0, 0, 0)),
            pl.BlockSpec(t_lo.shape, lambda i, o, a, l: (0, 0, 0)),
        ],
        out_specs=pl.BlockSpec((ROW_TILE, AB_DEV), lambda i, o, a, l: (i, 0)),
        scratch_shapes=[pltpu.VMEM((ab_blocks, ROW_TILE, BLK), jnp.float32)],
    )
    return pl.pallas_call(
        make_kernel(ncd, per_cd, ab_blocks),
        grid_spec=grid_spec,
        out_shape=jax.ShapeDtypeStruct((rows, AB_DEV), jnp.float32),
    )(order, ab_sorted, live_sorted, amp3, t_hi, t_lo)


def on_device(amplitudes, integral_tiles, tile_cd, tile_ab, tile_count):
    rows, cd = amplitudes.shape
    local = amplitudes.reshape(rows, cd // BLK, BLK).transpose(1, 0, 2)
    amp3 = lax.all_gather(local, ("row", "col"), axis=1, tiled=True)
    return sparse_ladder(amp3, integral_tiles, tile_cd, tile_ab, tile_count[0])


def solution(mesh):
    placed = (
        P(("row", "col"), None),
        P(("row", "col"), None, None),
        P(("row", "col")),
        P(("row", "col")),
        P(("row", "col")),
    )
    return jax.shard_map(
        on_device, mesh=mesh, in_specs=placed, out_specs=P(None, ("row", "col")), check_vma=False
    )
```

```python
import jax
import jax.numpy as jnp
from jax import lax
from jax.experimental import pallas as pl
from jax.experimental.pallas import tpu as pltpu
from jax.sharding import PartitionSpec as P

BLK = 128
AB_DEV = 2048
SLOTS = 32
ROW_TILE = 256


def split_f32(x):
    hi = x.astype(jnp.bfloat16)
    return hi, (x - hi.astype(jnp.float32)).astype(jnp.bfloat16)


def split_tiles(x):
    hi = lax.reduce_precision(x, exponent_bits=8, mantissa_bits=7)
    return hi.astype(jnp.bfloat16), (x - hi).astype(jnp.bfloat16)


def make_kernel(ncd, ab_blocks, per_ab):
    def dot(x, y):
        return jnp.dot(x, y, preferred_element_type=jnp.float32)

    def ladder_kernel(order_ref, cd_ref, live_ref, amp_ref, hi_ref, lo_ref, out_ref, ahi_ref, alo_ref):
        for c in range(ncd):
            a_hi, a_lo = split_f32(amp_ref[c])
            ahi_ref[c] = a_hi
            alo_ref[c] = a_lo
        for j in range(ab_blocks):
            acc = None
            for k in range(per_ab):
                idx = j * per_ab + k
                c = cd_ref[idx]
                s = order_ref[idx]
                a_hi = ahi_ref[c]
                t_hi = hi_ref[s]
                part = dot(a_hi, t_hi) + (dot(a_hi, lo_ref[s]) + dot(alo_ref[c], t_hi))
                part = jnp.where(live_ref[idx] > 0, part, 0.0)
                acc = part if acc is None else acc + part
            out_ref[:, j * BLK:(j + 1) * BLK] = acc

    return ladder_kernel


def slot_tables(tile_cd, tile_ab, count):
    n = tile_ab.shape[0]
    slot = jnp.arange(n, dtype=jnp.int32)
    key = tile_ab.astype(jnp.int32) * n + slot
    rank = jnp.sum((key[None, :] < key[:, None]).astype(jnp.int32), axis=1)
    hit = rank[None, :] == slot[:, None]
    order = jnp.sum(jnp.where(hit, slot[None, :], 0), axis=1)
    cd_sorted = jnp.sum(jnp.where(hit, tile_cd[None, :].astype(jnp.int32), 0), axis=1)
    live_sorted = (order < count).astype(jnp.int32)
    return order, cd_sorted, live_sorted


def sparse_ladder(amp3, tiles, tile_cd, tile_ab, count):
    ncd, rows, _ = amp3.shape
    ab_blocks = AB_DEV // BLK
    per_ab = SLOTS // ab_blocks
    order, cd_sorted, live_sorted = slot_tables(tile_cd, tile_ab, count)
    t_hi, t_lo = split_tiles(tiles)
    grid_spec = pltpu.PrefetchScalarGridSpec(
        num_scalar_prefetch=3,
        grid=(rows // ROW_TILE,),
        in_specs=[
            pl.BlockSpec((ncd, ROW_TILE, BLK), lambda i, o, c, l: (0, i, 0)),
            pl.BlockSpec(t_hi.shape, lambda i, o, c, l: (0, 0, 0)),
            pl.BlockSpec(t_lo.shape, lambda i, o, c, l: (0, 0, 0)),
        ],
        out_specs=pl.BlockSpec((ROW_TILE, AB_DEV), lambda i, o, c, l: (i, 0)),
        scratch_shapes=[
            pltpu.VMEM((ncd, ROW_TILE, BLK), jnp.bfloat16),
            pltpu.VMEM((ncd, ROW_TILE, BLK), jnp.bfloat16),
        ],
    )
    return pl.pallas_call(
        make_kernel(ncd, ab_blocks, per_ab),
        grid_spec=grid_spec,
        out_shape=jax.ShapeDtypeStruct((rows, AB_DEV), jnp.float32),
    )(order, cd_sorted, live_sorted, amp3, t_hi, t_lo)


def on_device(amplitudes, integral_tiles, tile_cd, tile_ab, tile_count):
    rows, cd = amplitudes.shape
    local = amplitudes.reshape(rows, cd // BLK, BLK).transpose(1, 0, 2)
    amp3 = lax.all_gather(local, ("row", "col"), axis=1, tiled=True)
    return sparse_ladder(amp3, integral_tiles, tile_cd, tile_ab, tile_count[0])


def solution(mesh):
    placed = (
        P(("row", "col"), None),
        P(("row", "col"), None, None),
        P(("row", "col")),
        P(("row", "col")),
        P(("row", "col")),
    )
    return jax.shard_map(
        on_device, mesh=mesh, in_specs=placed, out_specs=P(None, ("row", "col")), check_vma=False
    )
```

```python
import jax
import jax.numpy as jnp
from jax import lax
from jax.experimental import pallas as pl
from jax.experimental.pallas import tpu as pltpu
from jax.sharding import PartitionSpec as P

BLK = 128
AB_DEV = 2048
SLOTS = 32
ROW_TILE = 512


def split_f32(x):
    hi = x.astype(jnp.bfloat16)
    return hi, (x - hi.astype(jnp.float32)).astype(jnp.bfloat16)


def split_outside(x):
    hi = lax.reduce_precision(x, exponent_bits=8, mantissa_bits=7)
    return hi.astype(jnp.bfloat16), (x - hi).astype(jnp.bfloat16)


def make_kernel(groups):
    def dot(x, y):
        return jnp.dot(x, y, preferred_element_type=jnp.float32)

    def ladder_kernel(cd_ref, ab_ref, amp_ref, whi_ref, wlo_ref, out_ref):
        for g in range(groups):
            lhs = jnp.concatenate([amp_ref[cd_ref[2 * g]], amp_ref[cd_ref[2 * g + 1]]], axis=1)
            l_hi, l_lo = split_f32(lhs)
            w_hi = whi_ref[g]
            res = dot(l_hi, w_hi) + (dot(l_hi, wlo_ref[g]) + dot(l_lo, w_hi))
            for k in range(2):
                col = pl.multiple_of(ab_ref[2 * g + k] * BLK, BLK)
                out_ref[:, pl.ds(col, BLK)] = res[:, k * BLK:(k + 1) * BLK]

    return ladder_kernel


def rank_order(key):
    n = key.shape[0]
    idx = jnp.arange(n, dtype=jnp.int32)
    rank = jnp.sum((key[None, :] < key[:, None]).astype(jnp.int32), axis=1)
    return jnp.sum(jnp.where(rank[None, :] == idx[:, None], idx[None, :], 0), axis=1)


def label_tables(tiles, tile_cd, tile_ab, count):
    n = tile_ab.shape[0]
    ab_blocks = AB_DEV // BLK
    slot = jnp.arange(n, dtype=jnp.int32)
    cd = tile_cd.astype(jnp.int32)
    ab = tile_ab.astype(jnp.int32)
    by_ab = rank_order(ab * (n * n) + cd * n + slot)
    cd_of = cd[by_ab].reshape(ab_blocks, 2)
    slot_of = by_ab.reshape(ab_blocks, 2)
    blocks = jnp.arange(ab_blocks, dtype=jnp.int32)
    pair = rank_order(cd_of[:, 0] * ab_blocks + blocks).reshape(-1, 2)
    ab_tab = pair.reshape(-1)
    cd_tab = cd_of[pair[:, 0]].reshape(-1)
    masked = jnp.where((slot < count)[:, None, None], tiles, 0.0)
    t = masked[slot_of[pair]]
    w = t.transpose(0, 2, 3, 1, 4).reshape(-1, 2 * BLK, 2 * BLK)
    return cd_tab, ab_tab, w


def sparse_ladder(amp3, tiles, tile_cd, tile_ab, count):
    ncd, rows, _ = amp3.shape
    cd_tab, ab_tab, w = label_tables(tiles, tile_cd, tile_ab, count)
    w_hi, w_lo = split_outside(w)
    groups = w.shape[0]
    grid_spec = pltpu.PrefetchScalarGridSpec(
        num_scalar_prefetch=2,
        grid=(rows // ROW_TILE,),
        in_specs=[
            pl.BlockSpec((ncd, ROW_TILE, BLK), lambda i, c, a: (0, i, 0)),
            pl.BlockSpec(w_hi.shape, lambda i, c, a: (0, 0, 0)),
            pl.BlockSpec(w_lo.shape, lambda i, c, a: (0, 0, 0)),
        ],
        out_specs=pl.BlockSpec((ROW_TILE, AB_DEV), lambda i, c, a: (i, 0)),
    )
    return pl.pallas_call(
        make_kernel(groups),
        grid_spec=grid_spec,
        out_shape=jax.ShapeDtypeStruct((rows, AB_DEV), jnp.float32),
    )(cd_tab, ab_tab, amp3, w_hi, w_lo)


def on_device(amplitudes, integral_tiles, tile_cd, tile_ab, tile_count):
    rows, cd = amplitudes.shape
    local = amplitudes.reshape(rows, cd // BLK, BLK).transpose(1, 0, 2)
    amp3 = lax.all_gather(local, ("row", "col"), axis=1, tiled=True)
    return sparse_ladder(amp3, integral_tiles, tile_cd, tile_ab, tile_count[0])


def solution(mesh):
    placed = (
        P(("row", "col"), None),
        P(("row", "col"), None, None),
        P(("row", "col")),
        P(("row", "col")),
        P(("row", "col")),
    )
    return jax.shard_map(
        on_device, mesh=mesh, in_specs=placed, out_specs=P(None, ("row", "col")), check_vma=False
    )
```
